256 devices in a mesh: dp: 4 (over y_lo, core), block: 64 (over x, y_hi, z).
Axes of the slice: x: 4, y: 4 (y_hi: 2, y_lo: 2; y = y_hi * 2 + y_lo), z: 8, core: 2. Of those that a mesh axis runs over, the one named last changes fastest.
Arguments:
- tokens: bfloat16 [4096, 16384], P('dp', 'block'), may hold values from -6 to 6
- cotangent: bfloat16 [4096, 16384], P('dp', 'block'), may hold values from -6 to 6
- up_width: bfloat16 [64, 256, 1024], P('block'), may hold values from -0.375 to 0.375
- up_hidden: bfloat16 [256, 256, 256], P('block'), may hold values from -0.375 to 0.375
- down_hidden: bfloat16 [256, 256, 256], P('block'), may hold values from -0.375 to 0.375
- down_width: bfloat16 [64, 1024, 256], P('block'), may hold values from -0.1875 to 0.1875
Outputs:
- layer_out: bfloat16 [4096, 16384], P('dp', 'block')
- tokens_grad: bfloat16 [4096, 16384], P('dp', 'block')
- up_width_grad: float32 [64, 256, 1024], P('block')
- up_hidden_grad: float32 [256, 256, 256], P('block')
- down_hidden_grad: float32 [256, 256, 256], P('block')
- down_width_grad: float32 [64, 1024, 256], P('block')
The draws below stay inside these ranges and needn't reach their ends.
All inputs are finite; a program needn't handle non-finite values.
Results may differ from the reference program's by a relative error of at most 0.014.
Values may be sent and summed in bfloat16 or wider, within the bound.
No kernel may reach another device: no remote copies, remote signals or barrier semaphores. Data moves between devices by JAX's collectives and lax.ppermute only.
A program may use at most 64 MiB of HBM per device.

```python
import math
import jax
import jax.numpy as jnp
from jax import lax

BS = 256
Q = 4
TOKENS = 4096
D = 16384
G = 256
N_BLOCK = 64


def level_of(stream_key, extent, cuts, smallest, top_value):
    factor_of, own = 1.0, jax.random.fold_in(stream_key, 6)
    for position, blocks in cuts:
        steps = jnp.exp(jax.random.uniform(jax.random.fold_in(own, position), (blocks,), jnp.float32, smallest / len(cuts), top_value / len(cuts)))
        factor_of = factor_of * jnp.repeat(steps, extent[position] // blocks).reshape([-1 if axis == position else 1 for axis in range(len(extent))])
    return factor_of


def gaussian(key, extent, spread, limit, cuts=(), kind=jnp.bfloat16):
    entries = spread * jax.random.normal(key, extent, jnp.float32)
    if cuts:
        entries = entries * level_of(key, extent, cuts, -0.22, 0.18)
    return jnp.clip(entries, -limit, limit).astype(kind)


def setup_inputs(seed: int = 0) -> dict:
    key_of = jax.random.split(jax.random.key(seed), 7)
    tokens = gaussian(key_of[0], (TOKENS, D), 1.0, 6.0, ((0, 4), (1, 64)))
    cotangent = gaussian(key_of[1], (TOKENS, D), 1.0, 6.0, ((0, 4), (1, 64)))
    up_width = gaussian(key_of[2], (N_BLOCK, BS, Q * BS), BS ** -0.5, 0.375, ((0, 64),))
    up_hidden = gaussian(key_of[3], (BS, G, G), G ** -0.5, 0.375, ((0, 64),))
    down_hidden = gaussian(key_of[4], (BS, G, G), G ** -0.5, 0.375, ((0, 64),))
    down_width = gaussian(key_of[5], (N_BLOCK, Q * BS, BS), (Q * BS) ** -0.5, 0.1875, ((0, 64),))
    return dict(tokens=tokens, cotangent=cotangent, up_width=up_width, up_hidden=up_hidden, down_hidden=down_hidden, down_width=down_width)


def gelu_exact(value):
    return 0.5 * value * (1.0 + jax.scipy.special.erf(value / math.sqrt(2.0)))

def gelu_slope(value):
    return 0.5 * (1.0 + jax.scipy.special.erf(value / math.sqrt(2.0))) + value * jnp.exp(-0.5 * value * value) / math.sqrt(2.0 * math.pi)

def reference(tokens, cotangent, up_width, up_hidden, down_hidden, down_width):
    block_rows = min(512, TOKENS)
    block_count = TOKENS // block_rows
    token_blocks = tokens.reshape(block_count, block_rows, N_BLOCK, BS)
    cot_blocks = cotangent.reshape(block_count, block_rows, N_BLOCK, BS)
    uw32 = up_width.astype(jnp.float32)
    uh32 = up_hidden.astype(jnp.float32)
    dh32 = down_hidden.astype(jnp.float32)
    dw32 = down_width.astype(jnp.float32)

    def one_block(carry, inputs):
        grad_uw, grad_uh, grad_dh, grad_dw = carry
        x_block, c_block = inputs
        x32 = x_block.astype(jnp.float32)
        c32 = c_block.astype(jnp.float32)
        h_full = jnp.einsum('rbi,bic->rbc', x32, uw32).astype(jnp.bfloat16)
        z_full = h_full.reshape(block_rows, N_BLOCK, BS, Q).transpose(0, 2, 1, 3).reshape(block_rows, BS, G)
        pre_act = jnp.einsum('rkg,kgm->rkm', z_full.astype(jnp.float32), uh32)
        active = gelu_exact(pre_act).astype(jnp.bfloat16)
        e_full = jnp.einsum('rkm,kmn->rkn', active.astype(jnp.float32), dh32).astype(jnp.bfloat16)
        f_full = e_full.reshape(block_rows, BS, N_BLOCK, Q).transpose(0, 2, 1, 3).reshape(block_rows, N_BLOCK, BS * Q)
        layer_out = jnp.einsum('rbc,bco->rbo', f_full.astype(jnp.float32), dw32).astype(jnp.bfloat16)
        df_full = jnp.einsum('rbo,bco->rbc', c32, dw32).astype(jnp.bfloat16)
        grad_dw = grad_dw + jnp.einsum('rbc,rbo->bco', f_full.astype(jnp.float32), c32)
        de_full = df_full.reshape(block_rows, N_BLOCK, BS, Q).transpose(0, 2, 1, 3).reshape(block_rows, BS, G)
        de32 = de_full.astype(jnp.float32)
        grad_dh = grad_dh + jnp.einsum('rkm,rkn->kmn', active.astype(jnp.float32), de32)
        act_grad = jnp.einsum('rkn,kmn->rkm', de32, dh32)
        pre_grad = (act_grad * gelu_slope(pre_act)).astype(jnp.bfloat16)
        grad_uh = grad_uh + jnp.einsum('rkg,rkm->kgm', z_full.astype(jnp.float32), pre_grad.astype(jnp.float32))
        dz_full = jnp.einsum('rkm,kgm->rkg', pre_grad.astype(jnp.float32), uh32).astype(jnp.bfloat16)
        dh_full = dz_full.reshape(block_rows, BS, N_BLOCK, Q).transpose(0, 2, 1, 3).reshape(block_rows, N_BLOCK, BS * Q)
        grad_uw = grad_uw + jnp.einsum('rbi,rbc->bic', x32, dh_full.astype(jnp.float32))
        input_grad = jnp.einsum('rbc,bic->rbi', dh_full.astype(jnp.float32), uw32).astype(jnp.bfloat16)
        return ((grad_uw, grad_uh, grad_dh, grad_dw), (layer_out, input_grad))
    start = (jnp.zeros((N_BLOCK, BS, Q * BS), jnp.float32), jnp.zeros((BS, G, G), jnp.float32), jnp.zeros((BS, G, G), jnp.float32), jnp.zeros((N_BLOCK, Q * BS, BS), jnp.float32))
    totals, (outs, grads) = lax.scan(one_block, start, (token_blocks, cot_blocks))
    grad_scale = 1.0 / math.sqrt(TOKENS)
    return (outs.reshape(TOKENS, N_BLOCK * BS), grads.reshape(TOKENS, N_BLOCK * BS), totals[0] * grad_scale, totals[1] * grad_scale, totals[2] * grad_scale, totals[3] * grad_scale)
```

```python
import math

import jax
import jax.numpy as jnp
from jax import lax
from jax.sharding import PartitionSpec as P


def gelu_exact(value):
    return 0.5 * value * (1.0 + jax.scipy.special.erf(value / math.sqrt(2.0)))


def gelu_slope(value):
    return 0.5 * (1.0 + jax.scipy.special.erf(value / math.sqrt(2.0))) + value * jnp.exp(
        -0.5 * value * value
    ) / math.sqrt(2.0 * math.pi)


def dot(left, right, left_dims, right_dims, batch=((), ())):
    return lax.dot_general(
        left, right, ((left_dims, right_dims), batch), preferred_element_type=jnp.float32
    )


def shards(tokens, cotangent, up_width, up_hidden, down_hidden, down_width):
    row_count, block_size = tokens.shape
    nb = lax.axis_size("block")
    local_blocks, hidden_size, _ = up_hidden.shape
    expand = up_width.shape[2] // block_size
    chunk = local_blocks * expand
    grad_scale = 1.0 / math.sqrt(row_count * lax.axis_size("dp"))
    uw = up_width[0]
    dw = down_width[0]

    expanded_t = dot(uw, tokens, (0,), (1,)).astype(jnp.bfloat16)
    out_grad_t = dot(dw, cotangent, (1,), (1,)).astype(jnp.bfloat16)
    send = jnp.stack(
        [expanded_t.reshape(nb, chunk, row_count), out_grad_t.reshape(nb, chunk, row_count)], axis=1
    )
    recv = lax.all_to_all(send, "block", 0, 0, tiled=True)
    recv = recv.reshape(nb, 2, local_blocks, expand, row_count)
    hidden_t = recv[:, 0].transpose(1, 0, 2, 3).reshape(local_blocks, nb * expand, row_count)
    grad_t = recv[:, 1].transpose(1, 0, 2, 3).reshape(local_blocks, nb * expand, row_count)

    pre_act = dot(up_hidden, hidden_t, (1,), (1,), ((0,), (0,)))
    active = gelu_exact(pre_act).astype(jnp.bfloat16)
    back_t = dot(down_hidden, active, (1,), (1,), ((0,), (0,))).astype(jnp.bfloat16)
    act_grad = dot(down_hidden, grad_t, (2,), (1,), ((0,), (0,)))
    pre_grad = (act_grad * gelu_slope(pre_act)).astype(jnp.bfloat16)
    tile_grad_t = dot(up_hidden, pre_grad, (2,), (1,), ((0,), (0,))).astype(jnp.bfloat16)
    down_hidden_grad = dot(active, grad_t, (2,), (2,), ((0,), (0,)))
    up_hidden_grad = dot(hidden_t, pre_grad, (2,), (2,), ((0,), (0,)))
    dhg = lax.psum(down_hidden_grad.astype(jnp.bfloat16), "dp").astype(jnp.float32)
    uhg = lax.psum(up_hidden_grad.astype(jnp.bfloat16), "dp").astype(jnp.float32)

    send2 = jnp.stack([back_t, tile_grad_t], axis=0).reshape(2, local_blocks, nb, expand, row_count)
    send2 = send2.transpose(2, 0, 1, 3, 4)
    recv2 = lax.all_to_all(send2, "block", 0, 0, tiled=True)
    rows_t = recv2[:, 0].reshape(nb * chunk, row_count)
    rows_grad_t = recv2[:, 1].reshape(nb * chunk, row_count)

    layer_out = dot(rows_t, dw, (0,), (0,)).astype(jnp.bfloat16)
    down_width_grad = dot(rows_t, cotangent, (1,), (0,))
    tokens_grad = dot(rows_grad_t, uw, (0,), (1,)).astype(jnp.bfloat16)
    up_width_grad = dot(tokens, rows_grad_t, (0,), (1,))
    dwg = lax.psum(down_width_grad.astype(jnp.bfloat16), "dp").astype(jnp.float32)
    uwg = lax.psum(up_width_grad.astype(jnp.bfloat16), "dp").astype(jnp.float32)
    return (
        layer_out,
        tokens_grad,
        (uwg * grad_scale)[None],
        uhg * grad_scale,
        dhg * grad_scale,
        (dwg * grad_scale)[None],
    )


def solution(mesh):
    in_specs = (
        P("dp", "block"),
        P("dp", "block"),
        P("block", None, None),
        P("block", None, None),
        P("block", None, None),
        P("block", None, None),
    )
    out_specs = in_specs
    return jax.shard_map(shards, mesh=mesh, in_specs=in_specs, out_specs=out_specs, check_vma=False)
```

```python
import math

import jax
import jax.numpy as jnp
from jax import lax
from jax.sharding import PartitionSpec as P

CHUNKS = 2


def gelu_exact(value):
    return 0.5 * value * (1.0 + jax.scipy.special.erf(value / math.sqrt(2.0)))


def gelu_slope(value):
    return 0.5 * (1.0 + jax.scipy.special.erf(value / math.sqrt(2.0))) + value * jnp.exp(
        -0.5 * value * value
    ) / math.sqrt(2.0 * math.pi)


def dot(left, right, left_dims, right_dims, batch=((), ())):
    return lax.dot_general(
        left, right, ((left_dims, right_dims), batch), preferred_element_type=jnp.float32
    )


def pick(pair, index):
    return lax.dynamic_index_in_dim(pair, index, axis=0, keepdims=False)


def dp_sum(grad):
    size = lax.axis_size("dp")
    index = lax.axis_index("dp")
    core = index % 2
    row = index // 2
    core_swap = [(i, i ^ 1) for i in range(size)]
    row_swap = [(i, i ^ 2) for i in range(size)]
    parts = grad.astype(jnp.bfloat16).reshape(2, 2, -1)
    got = lax.ppermute(pick(parts, 1 - core), "dp", core_swap)
    half = pick(parts, core).astype(jnp.float32) + got.astype(jnp.float32)
    got = lax.ppermute(pick(half, 1 - row).astype(jnp.bfloat16), "dp", row_swap)
    quarter = (pick(half, row) + got.astype(jnp.float32)).astype(jnp.bfloat16)
    got = lax.ppermute(quarter, "dp", row_swap)
    half = jnp.where(row == 0, jnp.stack([quarter, got]), jnp.stack([got, quarter]))
    got = lax.ppermute(half, "dp", core_swap)
    full = jnp.where(core == 0, jnp.stack([half, got]), jnp.stack([got, half]))
    return full.reshape(grad.shape).astype(jnp.float32)


def shards(tokens, cotangent, up_width, up_hidden, down_hidden, down_width):
    total_rows, block_size = tokens.shape
    nb = lax.axis_size("block")
    local_blocks = up_hidden.shape[0]
    expand = up_width.shape[2] // block_size
    chunk = local_blocks * expand
    grad_scale = 1.0 / math.sqrt(total_rows * lax.axis_size("dp"))
    uw = up_width[0]
    dw = down_width[0]
    rows = total_rows // CHUNKS

    outs, tgrads = [], []
    dhg = uhg = dwg = uwg = None
    for step in range(CHUNKS):
        x = tokens[step * rows:(step + 1) * rows]
        c = cotangent[step * rows:(step + 1) * rows]
        expanded_t = dot(uw, x, (0,), (1,)).astype(jnp.bfloat16)
        out_grad_t = dot(dw, c, (1,), (1,)).astype(jnp.bfloat16)
        send = jnp.stack(
            [expanded_t.reshape(nb, chunk, rows), out_grad_t.reshape(nb, chunk, rows)], axis=1
        )
        recv = lax.all_to_all(send, "block", 0, 0, tiled=True)
        recv = recv.reshape(nb, 2, local_blocks, expand, rows)
        hidden_t = recv[:, 0].transpose(1, 0, 2, 3).reshape(local_blocks, nb * expand, rows)
        grad_t = recv[:, 1].transpose(1, 0, 2, 3).reshape(local_blocks, nb * expand, rows)

        pre_act = dot(up_hidden, hidden_t, (1,), (1,), ((0,), (0,)))
        active = gelu_exact(pre_act).astype(jnp.bfloat16)
        back_t = dot(down_hidden, active, (1,), (1,), ((0,), (0,))).astype(jnp.bfloat16)
        act_grad = dot(down_hidden, grad_t, (2,), (1,), ((0,), (0,)))
        pre_grad = (act_grad * gelu_slope(pre_act)).astype(jnp.bfloat16)
        tile_grad_t = dot(up_hidden, pre_grad, (2,), (1,), ((0,), (0,))).astype(jnp.bfloat16)
        g_dh = dot(active, grad_t, (2,), (2,), ((0,), (0,)))
        g_uh = dot(hidden_t, pre_grad, (2,), (2,), ((0,), (0,)))
        dhg = g_dh if dhg is None else dhg + g_dh
        uhg = g_uh if uhg is None else uhg + g_uh

        send2 = jnp.stack([back_t, tile_grad_t], axis=0).reshape(2, local_blocks, nb, expand, rows)
        send2 = send2.transpose(2, 0, 1, 3, 4)
        recv2 = lax.all_to_all(send2, "block", 0, 0, tiled=True)
        rows_t = recv2[:, 0].reshape(nb * chunk, rows)
        rows_grad_t = recv2[:, 1].reshape(nb * chunk, rows)

        outs.append(dot(rows_t, dw, (0,), (0,)).astype(jnp.bfloat16))
        tgrads.append(dot(rows_grad_t, uw, (0,), (1,)).astype(jnp.bfloat16))
        g_dw = dot(rows_t, c, (1,), (0,))
        g_uw = dot(x, rows_grad_t, (0,), (1,))
        dwg = g_dw if dwg is None else dwg + g_dw
        uwg = g_uw if uwg is None else uwg + g_uw

    dhg = dp_sum(dhg)
    uhg = dp_sum(uhg)
    dwg = dp_sum(dwg)
    uwg = dp_sum(uwg)
    return (
        jnp.concatenate(outs, axis=0),
        jnp.concatenate(tgrads, axis=0),
        (uwg * grad_scale)[None],
        uhg * grad_scale,
        dhg * grad_scale,
        (dwg * grad_scale)[None],
    )


def solution(mesh):
    in_specs = (
        P("dp", "block"),
        P("dp", "block"),
        P("block", None, None),
        P("block", None, None),
        P("block", None, None),
        P("block", None, None),
    )
    out_specs = in_specs
    return jax.shard_map(shards, mesh=mesh, in_specs=in_specs, out_specs=out_specs, check_vma=False)
```

```python
import math

import jax
import jax.numpy as jnp
from jax import lax
from jax.sharding import PartitionSpec as P

GROUPS = 2


def gelu_exact(value):
    return 0.5 * value * (1.0 + jax.scipy.special.erf(value / math.sqrt(2.0)))


def gelu_slope(value):
    return 0.5 * (1.0 + jax.scipy.special.erf(value / math.sqrt(2.0))) + value * jnp.exp(
        -0.5 * value * value
    ) / math.sqrt(2.0 * math.pi)


def dot(left, right, left_dims, right_dims, batch=((), ())):
    return lax.dot_general(
        left, right, ((left_dims, right_dims), batch), preferred_element_type=jnp.float32
    )


def pick(pair, index):
    return lax.dynamic_index_in_dim(pair, index, axis=0, keepdims=False)


def dp_sum(flat):
    size = lax.axis_size("dp")
    index = lax.axis_index("dp")
    core = index % 2
    row = index // 2
    core_swap = [(i, i ^ 1) for i in range(size)]
    row_swap = [(i, i ^ 2) for i in range(size)]
    parts = flat.reshape(2, 2, -1)
    got = lax.ppermute(pick(parts, 1 - core), "dp", core_swap)
    half = pick(parts, core).astype(jnp.float32) + got.astype(jnp.float32)
    got = lax.ppermute(pick(half, 1 - row).astype(jnp.bfloat16), "dp", row_swap)
    quarter = (pick(half, row) + got.astype(jnp.float32)).astype(jnp.bfloat16)
    got = lax.ppermute(quarter, "dp", row_swap)
    half = jnp.where(row == 0, jnp.stack([quarter, got]), jnp.stack([got, quarter]))
    got = lax.ppermute(half, "dp", core_swap)
    full = jnp.where(core == 0, jnp.stack([half, got]), jnp.stack([got, half]))
    return full.reshape(-1)


def summed(scale, *grads):
    flat = jnp.concatenate([(g * scale).astype(jnp.bfloat16).reshape(-1) for g in grads])
    total = dp_sum(flat).astype(jnp.float32)
    out, start = [], 0
    for g in grads:
        out.append(total[start:start + g.size].reshape(g.shape))
        start += g.size
    return out


def shards(tokens, cotangent, up_width, up_hidden, down_hidden, down_width):
    rows, block_size = tokens.shape
    nb = lax.axis_size("block")
    local_blocks, hidden_size, _ = up_hidden.shape
    expand = up_width.shape[2] // block_size
    per = local_blocks // GROUPS
    grad_scale = 1.0 / math.sqrt(rows * lax.axis_size("dp"))
    uw = up_width[0].reshape(block_size, nb, GROUPS, per * expand)
    dw = down_width[0].reshape(nb, GROUPS, per * expand, block_size)

    out_acc = tg_acc = None
    dhg, uhg, dwg, uwg = [], [], [], []
    for grp in range(GROUPS):
        uw_g = uw[:, :, grp].reshape(block_size, nb * per * expand)
        dw_g = dw[:, grp].reshape(nb * per * expand, block_size)
        expanded_t = dot(uw_g, tokens, (0,), (1,)).astype(jnp.bfloat16)
        out_grad_t = dot(dw_g, cotangent, (1,), (1,)).astype(jnp.bfloat16)
        send = jnp.stack(
            [expanded_t.reshape(nb, per * expand, rows), out_grad_t.reshape(nb, per * expand, rows)],
            axis=1,
        )
        recv = lax.all_to_all(send, "block", 0, 0, tiled=True)
        recv = recv.reshape(nb, 2, per, expand, rows)
        hidden_t = recv[:, 0].transpose(1, 0, 2, 3).reshape(per, nb * expand, rows)
        grad_t = recv[:, 1].transpose(1, 0, 2, 3).reshape(per, nb * expand, rows)

        uh = up_hidden[grp * per:(grp + 1) * per]
        dh = down_hidden[grp * per:(grp + 1) * per]
        pre_act = dot(uh, hidden_t, (1,), (1,), ((0,), (0,)))
        active = gelu_exact(pre_act).astype(jnp.bfloat16)
        back_t = dot(dh, active, (1,), (1,), ((0,), (0,))).astype(jnp.bfloat16)
        act_grad = dot(dh, grad_t, (2,), (1,), ((0,), (0,)))
        pre_grad = (act_grad * gelu_slope(pre_act)).astype(jnp.bfloat16)
        tile_grad_t = dot(uh, pre_grad, (2,), (1,), ((0,), (0,))).astype(jnp.bfloat16)
        g_dh = dot(active, grad_t, (2,), (2,), ((0,), (0,)))
        g_uh = dot(hidden_t, pre_grad, (2,), (2,), ((0,), (0,)))
        s_dh, s_uh = summed(grad_scale, g_dh, g_uh)
        dhg.append(s_dh)
        uhg.append(s_uh)

        send2 = jnp.stack([back_t, tile_grad_t], axis=0).reshape(2, per, nb, expand, rows)
        send2 = send2.transpose(2, 0, 1, 3, 4).reshape(nb, 2, per * expand, rows)
        recv2 = lax.all_to_all(send2, "block", 0, 0, tiled=True)
        rows_t = recv2[:, 0].reshape(nb * per * expand, rows)
        rows_grad_t = recv2[:, 1].reshape(nb * per * expand, rows)

        part_out = dot(rows_t, dw_g, (0,), (0,))
        part_tg = dot(rows_grad_t, uw_g, (0,), (1,))
        out_acc = part_out if out_acc is None else out_acc + part_out
        tg_acc = part_tg if tg_acc is None else tg_acc + part_tg
        g_dw = dot(rows_t, cotangent, (1,), (0,))
        g_uw = dot(tokens, rows_grad_t, (0,), (1,))
        s_dw, s_uw = summed(grad_scale, g_dw, g_uw)
        dwg.append(s_dw.reshape(nb, 1, per * expand, block_size))
        uwg.append(s_uw.reshape(block_size, nb, 1, per * expand))

    return (
        out_acc.astype(jnp.bfloat16),
        tg_acc.astype(jnp.bfloat16),
        jnp.concatenate(uwg, axis=2).reshape(1, block_size, -1),
        jnp.concatenate(uhg, axis=0),
        jnp.concatenate(dhg, axis=0),
        jnp.concatenate(dwg, axis=1).reshape(1, -1, block_size),
    )


def solution(mesh):
    in_specs = (
        P("dp", "block"),
        P("dp", "block"),
        P("block", None, None),
        P("block", None, None),
        P("block", None, None),
        P("block", None, None),
    )
    out_specs = in_specs
    return jax.shard_map(shards, mesh=mesh, in_specs=in_specs, out_specs=out_specs, check_vma=False)
```

```python
import math

import jax
import jax.numpy as jnp
from jax import lax
from jax.sharding import PartitionSpec as P

CHUNKS = 2


def gelu_exact(value):
    return 0.5 * value * (1.0 + jax.scipy.special.erf(value / math.sqrt(2.0)))


def gelu_slope(value):
    return 0.5 * (1.0 + jax.scipy.special.erf(value / math.sqrt(2.0))) + value * jnp.exp(
        -0.5 * value * value
    ) / math.sqrt(2.0 * math.pi)


def dot(left, right, left_dims, right_dims, batch=((), ())):
    return lax.dot_general(
        left, right, ((left_dims, right_dims), batch), preferred_element_type=jnp.float32
    )


def pick(pair, index):
    return lax.dynamic_index_in_dim(pair, index, axis=0, keepdims=False)


def dp_sum(grad, scale):
    size = lax.axis_size("dp")
    index = lax.axis_index("dp")
    core = index % 2
    row = index // 2
    core_swap = [(i, i ^ 1) for i in range(size)]
    row_swap = [(i, i ^ 2) for i in range(size)]
    own = (grad * scale).astype(jnp.bfloat16)
    got = lax.ppermute(own, "dp", core_swap)
    pair = (own.astype(jnp.float32) + got.astype(jnp.float32)).astype(jnp.bfloat16).reshape(2, -1)
    mine = pick(pair, core)
    got = lax.ppermute(mine, "dp", row_swap)
    total = (mine.astype(jnp.float32) + got.astype(jnp.float32)).astype(jnp.bfloat16)
    got = lax.ppermute(total, "dp", core_swap)
    full = jnp.where(core == 0, jnp.stack([total, got]), jnp.stack([got, total]))
    return full.reshape(grad.shape).astype(jnp.float32)


def shards(tokens, cotangent, up_width, up_hidden, down_hidden, down_width):
    total_rows, block_size = tokens.shape
    nb = lax.axis_size("block")
    local_blocks = up_hidden.shape[0]
    expand = up_width.shape[2] // block_size
    chunk = local_blocks * expand
    grad_scale = 1.0 / math.sqrt(total_rows * lax.axis_size("dp"))
    uw = up_width[0]
    dw = down_width[0]
    rows = total_rows // CHUNKS

    outs, tgrads = [], []
    dhg = uhg = dwg = uwg = None
    for step in range(CHUNKS):
        x = tokens[step * rows:(step + 1) * rows]
        c = cotangent[step * rows:(step + 1) * rows]
        expanded_t = dot(uw, x, (0,), (1,)).astype(jnp.bfloat16)
        out_grad_t = dot(dw, c, (1,), (1,)).astype(jnp.bfloat16)
        send = jnp.stack(
            [expanded_t.reshape(nb, chunk, rows), out_grad_t.reshape(nb, chunk, rows)], axis=1
        )
        recv = lax.all_to_all(send, "block", 0, 0, tiled=True)
        recv = recv.reshape(nb, 2, local_blocks, expand, rows)
        hidden_t = recv[:, 0].transpose(1, 0, 2, 3).reshape(local_blocks, nb * expand, rows)
        grad_t = recv[:, 1].transpose(1, 0, 2, 3).reshape(local_blocks, nb * expand, rows)

        pre_act = dot(up_hidden, hidden_t, (1,), (1,), ((0,), (0,)))
        active = gelu_exact(pre_act).astype(jnp.bfloat16)
        back_t = dot(down_hidden, active, (1,), (1,), ((0,), (0,))).astype(jnp.bfloat16)
        act_grad = dot(down_hidden, grad_t, (2,), (1,), ((0,), (0,)))
        pre_grad = (act_grad * gelu_slope(pre_act)).astype(jnp.bfloat16)
        tile_grad_t = dot(up_hidden, pre_grad, (2,), (1,), ((0,), (0,))).astype(jnp.bfloat16)
        g_dh = dot(active, grad_t, (2,), (2,), ((0,), (0,)))
        g_uh = dot(hidden_t, pre_grad, (2,), (2,), ((0,), (0,)))
        dhg = g_dh if dhg is None else dhg + g_dh
        uhg = g_uh if uhg is None else uhg + g_uh

        send2 = jnp.stack([back_t, tile_grad_t], axis=0).reshape(2, local_blocks, nb, expand, rows)
        send2 = send2.transpose(2, 0, 1, 3, 4).reshape(nb, 2, chunk, rows)
        recv2 = lax.all_to_all(send2, "block", 0, 0, tiled=True)
        rows_t = recv2[:, 0].reshape(nb * chunk, rows)
        rows_grad_t = recv2[:, 1].reshape(nb * chunk, rows)

        outs.append(dot(rows_t, dw, (0,), (0,)).astype(jnp.bfloat16))
        tgrads.append(dot(rows_grad_t, uw, (0,), (1,)).astype(jnp.bfloat16))
        g_dw = dot(rows_t, c, (1,), (0,))
        g_uw = dot(x, rows_grad_t, (0,), (1,))
        dwg = g_dw if dwg is None else dwg + g_dw
        uwg = g_uw if uwg is None else uwg + g_uw

    dhg = dp_sum(dhg, grad_scale)
    uhg = dp_sum(uhg, grad_scale)
    dwg = dp_sum(dwg, grad_scale)
    uwg = dp_sum(uwg, grad_scale)
    return (
        jnp.concatenate(outs, axis=0),
        jnp.concatenate(tgrads, axis=0),
        uwg[None],
        uhg,
        dhg,
        dwg[None],
    )


def solution(mesh):
    in_specs = (
        P("dp", "block"),
        P("dp", "block"),
        P("block", None, None),
        P("block", None, None),
        P("block", None, None),
        P("block", None, None),
    )
    out_specs = in_specs
    return jax.shard_map(shards, mesh=mesh, in_specs=in_specs, out_specs=out_specs, check_vma=False)
```

```python
import math

import jax
import jax.numpy as jnp
from jax import lax
from jax.sharding import PartitionSpec as P

CHUNKS = 2


def gelu_exact(value):
    return 0.5 * value * (1.0 + jax.scipy.special.erf(value / math.sqrt(2.0)))


def gelu_slope(value):
    return 0.5 * (1.0 + jax.scipy.special.erf(value / math.sqrt(2.0))) + value * jnp.exp(
        -0.5 * value * value
    ) / math.sqrt(2.0 * math.pi)


def dot(left, right, left_dims, right_dims, batch=((), ())):
    return lax.dot_general(
        left, right, ((left_dims, right_dims), batch), preferred_element_type=jnp.float32
    )


def pick(pair, index):
    return lax.dynamic_index_in_dim(pair, index, axis=0, keepdims=False)


def dp_sum(grad, scale):
    size = lax.axis_size("dp")
    index = lax.axis_index("dp")
    core = index % 2
    row = index // 2
    core_swap = [(i, i ^ 1) for i in range(size)]
    row_swap = [(i, i ^ 2) for i in range(size)]
    own = (grad * scale).astype(jnp.bfloat16)
    got = lax.ppermute(own, "dp", core_swap)
    pair = (own.astype(jnp.float32) + got.astype(jnp.float32)).astype(jnp.bfloat16)
    pair = pair.reshape((2, grad.shape[0] // 2) + grad.shape[1:])
    mine = pick(pair, core)
    got = lax.ppermute(mine, "dp", row_swap)
    total = (mine.astype(jnp.float32) + got.astype(jnp.float32)).astype(jnp.bfloat16)
    got = lax.ppermute(total, "dp", core_swap)
    full = jnp.where(core == 0, jnp.stack([total, got]), jnp.stack([got, total]))
    return full.astype(jnp.float32).reshape(grad.shape)


def shards(tokens, cotangent, up_width, up_hidden, down_hidden, down_width):
    total_rows, block_size = tokens.shape
    nb = lax.axis_size("block")
    local_blocks = up_hidden.shape[0]
    expand = up_width.shape[2] // block_size
    chunk = local_blocks * expand
    grad_scale = 1.0 / math.sqrt(total_rows * lax.axis_size("dp"))
    uw = up_width[0]
    dw = down_width[0]
    rows = total_rows // CHUNKS

    outs, tgrads = [], []
    dhg = uhg = dwg = uwg = None
    for step in range(CHUNKS):
        x = tokens[step * rows:(step + 1) * rows]
        c = cotangent[step * rows:(step + 1) * rows]
        expanded_t = dot(uw, x, (0,), (1,)).astype(jnp.bfloat16)
        out_grad_t = dot(dw, c, (1,), (1,)).astype(jnp.bfloat16)
        send = jnp.stack(
            [expanded_t.reshape(nb, chunk, rows), out_grad_t.reshape(nb, chunk, rows)], axis=1
        )
        recv = lax.all_to_all(send, "block", 0, 0, tiled=True)
        recv = recv.reshape(nb, 2, local_blocks, expand, rows)
        hidden_t = recv[:, 0].transpose(1, 0, 2, 3).reshape(local_blocks, nb * expand, rows)
        grad_t = recv[:, 1].transpose(1, 0, 2, 3).reshape(local_blocks, nb * expand, rows)

        pre_act = dot(up_hidden, hidden_t, (1,), (1,), ((0,), (0,)))
        active = gelu_exact(pre_act).astype(jnp.bfloat16)
        back_t = dot(down_hidden, active, (1,), (1,), ((0,), (0,))).astype(jnp.bfloat16)
        act_grad = dot(down_hidden, grad_t, (2,), (1,), ((0,), (0,)))
        pre_grad = (act_grad * gelu_slope(pre_act)).astype(jnp.bfloat16)
        tile_grad_t = dot(up_hidden, pre_grad, (2,), (1,), ((0,), (0,))).astype(jnp.bfloat16)
        g_dh = dot(active, grad_t, (2,), (2,), ((0,), (0,)))
        g_uh = dot(hidden_t, pre_grad, (2,), (2,), ((0,), (0,)))
        dhg = g_dh if dhg is None else dhg + g_dh
        uhg = g_uh if uhg is None else uhg + g_uh

        send2 = jnp.stack([back_t, tile_grad_t], axis=0).reshape(2, local_blocks, nb, expand, rows)
        send2 = send2.transpose(2, 0, 1, 3, 4).reshape(nb, 2, chunk, rows)
        recv2 = lax.all_to_all(send2, "block", 0, 0, tiled=True)
        rows_t = recv2[:, 0].reshape(nb * chunk, rows)
        rows_grad_t = recv2[:, 1].reshape(nb * chunk, rows)

        outs.append(dot(rows_t, dw, (0,), (0,)).astype(jnp.bfloat16))
        tgrads.append(dot(rows_grad_t, uw, (0,), (1,)).astype(jnp.bfloat16))
        g_dw = dot(rows_t, c, (1,), (0,))
        g_uw = dot(x, rows_grad_t, (0,), (1,))
        dwg = g_dw if dwg is None else dwg + g_dw
        uwg = g_uw if uwg is None else uwg + g_uw

    dhg = dp_sum(dhg, grad_scale)
    uhg = dp_sum(uhg, grad_scale)
    dwg = dp_sum(dwg, grad_scale)
    uwg = dp_sum(uwg, grad_scale)
    return (
        jnp.concatenate(outs, axis=0),
        jnp.concatenate(tgrads, axis=0),
        uwg[None],
        uhg,
        dhg,
        dwg[None],
    )


def solution(mesh):
    in_specs = (
        P("dp", "block"),
        P("dp", "block"),
        P("block", None, None),
        P("block", None, None),
        P("block", None, None),
        P("block", None, None),
    )
    out_specs = in_specs
    return jax.shard_map(shards, mesh=mesh, in_specs=in_specs, out_specs=out_specs, check_vma=False)
```

```python
import math

import jax
import jax.numpy as jnp
from jax import lax
from jax.sharding import PartitionSpec as P

CHUNKS = 2


def gelu_exact(value):
    return 0.5 * value * (1.0 + jax.scipy.special.erf(value / math.sqrt(2.0)))


def gelu_slope(value):
    return 0.5 * (1.0 + jax.scipy.special.erf(value / math.sqrt(2.0))) + value * jnp.exp(
        -0.5 * value * value
    ) / math.sqrt(2.0 * math.pi)


def dot(left, right, left_dims, right_dims, batch=((), ())):
    return lax.dot_general(
        left, right, ((left_dims, right_dims), batch), preferred_element_type=jnp.float32
    )


def pick(pair, index):
    return lax.dynamic_index_in_dim(pair, index, axis=0, keepdims=False)


def dp_sum(grad, scale):
    size = lax.axis_size("dp")
    index = lax.axis_index("dp")
    core = index % 2
    row = index // 2
    core_swap = [(i, i ^ 1) for i in range(size)]
    row_swap = [(i, i ^ 2) for i in range(size)]
    own = (grad * scale).astype(jnp.bfloat16)
    got = lax.ppermute(own, "dp", core_swap)
    pair = (own.astype(jnp.float32) + got.astype(jnp.float32)).astype(jnp.bfloat16)
    pair = pair.reshape((2, grad.shape[0] // 2) + grad.shape[1:])
    mine = pick(pair, core)
    got = lax.ppermute(mine, "dp", row_swap)
    total = (mine.astype(jnp.float32) + got.astype(jnp.float32)).astype(jnp.bfloat16)
    got = lax.ppermute(total, "dp", core_swap)
    full = jnp.where(core == 0, jnp.stack([total, got]), jnp.stack([got, total]))
    return full.astype(jnp.float32).reshape(grad.shape)


def shards(tokens, cotangent, up_width, up_hidden, down_hidden, down_width):
    total_rows, block_size = tokens.shape
    nb = lax.axis_size("block")
    local_blocks = up_hidden.shape[0]
    expand = up_width.shape[2] // block_size
    chunk = local_blocks * expand
    grad_scale = 1.0 / math.sqrt(total_rows * lax.axis_size("dp"))
    uw = up_width[0]
    dw = down_width[0]
    rows = total_rows // CHUNKS

    outs, tgrads = [], []
    dhg = uhg = dwg = uwg = None
    for step in range(CHUNKS):
        x = tokens[step * rows:(step + 1) * rows]
        c = cotangent[step * rows:(step + 1) * rows]
        expanded_t = dot(uw, x, (0,), (1,)).astype(jnp.bfloat16)
        out_grad_t = dot(dw, c, (1,), (1,)).astype(jnp.bfloat16)
        send = jnp.stack(
            [expanded_t.reshape(nb, chunk, rows), out_grad_t.reshape(nb, chunk, rows)], axis=1
        )
        recv = lax.all_to_all(send, "block", 0, 0, tiled=True)
        recv = recv.reshape(nb, 2, local_blocks, expand, rows)
        hidden_t = recv[:, 0].transpose(1, 0, 2, 3).reshape(local_blocks, nb * expand, rows)
        grad_t = recv[:, 1].transpose(1, 0, 2, 3).reshape(local_blocks, nb * expand, rows)

        pre_act = dot(up_hidden, hidden_t, (1,), (1,), ((0,), (0,)))
        active = gelu_exact(pre_act).astype(jnp.bfloat16)
        back_t = dot(down_hidden, active, (1,), (1,), ((0,), (0,))).astype(jnp.bfloat16)
        act_grad = dot(down_hidden, grad_t, (2,), (1,), ((0,), (0,)))
        pre_grad = (act_grad * gelu_slope(pre_act)).astype(jnp.bfloat16)
        tile_grad_t = dot(up_hidden, pre_grad, (2,), (1,), ((0,), (0,))).astype(jnp.bfloat16)
        g_dh = dot(active, grad_t, (2,), (2,), ((0,), (0,)))
        g_uh = dot(hidden_t, pre_grad, (2,), (2,), ((0,), (0,)))
        dhg = g_dh if dhg is None else dhg + g_dh
        uhg = g_uh if uhg is None else uhg + g_uh

        send2 = jnp.stack([back_t, tile_grad_t], axis=0).reshape(2, local_blocks, nb, expand, rows)
        send2 = send2.transpose(2, 0, 1, 3, 4).reshape(nb, 2, chunk, rows)
        recv2 = lax.all_to_all(send2, "block", 0, 0, tiled=True)
        rows_t = recv2[:, 0].reshape(nb * chunk, rows)
        rows_grad_t = recv2[:, 1].reshape(nb * chunk, rows)

        outs.append(dot(rows_t, dw, (0,), (0,)).astype(jnp.bfloat16))
        tgrads.append(dot(rows_grad_t, uw, (0,), (1,)).astype(jnp.bfloat16))
        g_dw = dot(rows_t, c, (1,), (0,))
        g_uw = dot(rows_grad_t, x, (1,), (0,))
        dwg = g_dw if dwg is None else dwg + g_dw
        uwg = g_uw if uwg is None else uwg + g_uw

    hidden_grads = dp_sum(jnp.stack([dhg, uhg]), grad_scale)
    width_grads = dp_sum(jnp.stack([dwg, uwg]), grad_scale)
    return (
        jnp.concatenate(outs, axis=0),
        jnp.concatenate(tgrads, axis=0),
        width_grads[1].T[None],
        hidden_grads[1],
        hidden_grads[0],
        width_grads[0][None],
    )


def solution(mesh):
    in_specs = (
        P("dp", "block"),
        P("dp", "block"),
        P("block", None, None),
        P("block", None, None),
        P("block", None, None),
        P("block", None, None),
    )
    out_specs = in_specs
    return jax.shard_map(shards, mesh=mesh, in_specs=in_specs, out_specs=out_specs, check_vma=False)
```

```python
import math

import jax
import jax.numpy as jnp
from jax import lax
from jax.sharding import PartitionSpec as P

CHUNKS = 2


def gelu_exact(value):
    return 0.5 * value * (1.0 + jax.scipy.special.erf(value / math.sqrt(2.0)))


def gelu_slope(value):
    return 0.5 * (1.0 + jax.scipy.special.erf(value / math.sqrt(2.0))) + value * jnp.exp(
        -0.5 * value * value
    ) / math.sqrt(2.0 * math.pi)


def dot(left, right, left_dims, right_dims, batch=((), ())):
    return lax.dot_general(
        left, right, ((left_dims, right_dims), batch), preferred_element_type=jnp.float32
    )


def pick(pair, index):
    return lax.dynamic_index_in_dim(pair, index, axis=0, keepdims=False)


def dp_sum(grad, scale, tied=None):
    size = lax.axis_size("dp")
    index = lax.axis_index("dp")
    core = index % 2
    row = index // 2
    core_swap = [(i, i ^ 1) for i in range(size)]
    row_swap = [(i, i ^ 2) for i in range(size)]
    own = (grad * scale).astype(jnp.bfloat16)
    got = lax.ppermute(own, "dp", core_swap)
    pair = (own.astype(jnp.float32) + got.astype(jnp.float32)).astype(jnp.bfloat16)
    if tied is not None:
        pair, tied = lax.optimization_barrier((pair, tied))
    pair = pair.reshape((2, grad.shape[0] // 2) + grad.shape[1:])
    mine = pick(pair, core)
    got = lax.ppermute(mine, "dp", row_swap)
    total = (mine.astype(jnp.float32) + got.astype(jnp.float32)).astype(jnp.bfloat16)
    got = lax.ppermute(total, "dp", core_swap)
    full = jnp.where(core == 0, jnp.stack([total, got]), jnp.stack([got, total]))
    return full.astype(jnp.float32).reshape(grad.shape), tied


def shards(tokens, cotangent, up_width, up_hidden, down_hidden, down_width):
    total_rows, block_size = tokens.shape
    nb = lax.axis_size("block")
    local_blocks = up_hidden.shape[0]
    expand = up_width.shape[2] // block_size
    chunk = local_blocks * expand
    grad_scale = 1.0 / math.sqrt(total_rows * lax.axis_size("dp"))
    uw = up_width[0]
    dw = down_width[0]
    rows = total_rows // CHUNKS

    outs, tgrads = [], []
    dhg = uhg = dwg = uwg = None
    for step in range(CHUNKS):
        x = tokens[step * rows:(step + 1) * rows]
        c = cotangent[step * rows:(step + 1) * rows]
        expanded_t = dot(uw, x, (0,), (1,)).astype(jnp.bfloat16)
        out_grad_t = dot(dw, c, (1,), (1,)).astype(jnp.bfloat16)
        send = jnp.stack(
            [expanded_t.reshape(nb, chunk, rows), out_grad_t.reshape(nb, chunk, rows)], axis=1
        )
        recv = lax.all_to_all(send, "block", 0, 0, tiled=True)
        recv = recv.reshape(nb, 2, local_blocks, expand, rows)
        hidden_t = recv[:, 0].transpose(1, 0, 2, 3).reshape(local_blocks, nb * expand, rows)
        grad_t = recv[:, 1].transpose(1, 0, 2, 3).reshape(local_blocks, nb * expand, rows)

        pre_act = dot(up_hidden, hidden_t, (1,), (1,), ((0,), (0,)))
        active = gelu_exact(pre_act).astype(jnp.bfloat16)
        back_t = dot(down_hidden, active, (1,), (1,), ((0,), (0,))).astype(jnp.bfloat16)
        act_grad = dot(down_hidden, grad_t, (2,), (1,), ((0,), (0,)))
        pre_grad = (act_grad * gelu_slope(pre_act)).astype(jnp.bfloat16)
        tile_grad_t = dot(up_hidden, pre_grad, (2,), (1,), ((0,), (0,))).astype(jnp.bfloat16)
        g_dh = dot(active, grad_t, (2,), (2,), ((0,), (0,)))
        g_uh = dot(hidden_t, pre_grad, (2,), (2,), ((0,), (0,)))
        dhg = g_dh if dhg is None else dhg + g_dh
        uhg = g_uh if uhg is None else uhg + g_uh

        send2 = jnp.stack([back_t, tile_grad_t], axis=0).reshape(2, local_blocks, nb, expand, rows)
        send2 = send2.transpose(2, 0, 1, 3, 4)
        if step < CHUNKS - 1:
            recv2 = lax.all_to_all(send2.reshape(nb, 2, chunk, rows), "block", 0, 0, tiled=True)
            rows_t = recv2[:, 0].reshape(nb * chunk, rows)
            rows_grad_t = recv2[:, 1].reshape(nb * chunk, rows)
            outs.append(dot(rows_t, dw, (0,), (0,)).astype(jnp.bfloat16))
            tgrads.append(dot(rows_grad_t, uw, (0,), (1,)).astype(jnp.bfloat16))
            g_dw = dot(rows_t, c, (1,), (0,))
            g_uw = dot(rows_grad_t, x, (1,), (0,))
            dwg = g_dw if dwg is None else dwg + g_dw
            uwg = g_uw if uwg is None else uwg + g_uw
            continue
        dw4 = dw.reshape(nb, local_blocks, expand, block_size)
        uw4 = uw.reshape(block_size, nb, local_blocks, expand)
        dwg4 = dwg.reshape(nb, local_blocks * expand, block_size)
        uwg4 = uwg.reshape(nb, local_blocks * expand, block_size)
        out_acc = tg_acc = None
        width_parts = []
        tail_payload = send2[:, :, local_blocks - 1:].reshape(nb, 2, expand, rows)
        for lo, hi in ((0, local_blocks - 1), (local_blocks - 1, local_blocks)):
            span = (hi - lo) * expand
            payload = send2[:, :, lo:hi].reshape(nb, 2, span, rows) if lo == 0 else tail_payload
            recv2 = lax.all_to_all(payload, "block", 0, 0, tiled=True)
            rows_t = recv2[:, 0].reshape(nb * span, rows)
            rows_grad_t = recv2[:, 1].reshape(nb * span, rows)
            dw_p = dw4[:, lo:hi].reshape(nb * span, block_size)
            uw_p = uw4[:, :, lo:hi].reshape(block_size, nb * span)
            part_out = dot(rows_t, dw_p, (0,), (0,))
            part_tg = dot(rows_grad_t, uw_p, (0,), (1,))
            out_acc = part_out if out_acc is None else out_acc + part_out
            tg_acc = part_tg if tg_acc is None else tg_acc + part_tg
            g_dw = dot(rows_t, c, (1,), (0,)).reshape(nb, span, block_size)
            g_uw = dot(rows_grad_t, x, (1,), (0,)).reshape(nb, span, block_size)
            g_dw = g_dw + dwg4[:, lo * expand:hi * expand]
            g_uw = g_uw + uwg4[:, lo * expand:hi * expand]
            if lo == 0:
                summed_part, tail_payload = dp_sum(jnp.stack([g_dw, g_uw]), grad_scale, tail_payload)
            else:
                summed_part = dp_sum(jnp.stack([g_dw, g_uw]), grad_scale)[0]
            width_parts.append(summed_part)
        outs.append(out_acc.astype(jnp.bfloat16))
        tgrads.append(tg_acc.astype(jnp.bfloat16))

    dhg = dp_sum(dhg, grad_scale)[0]
    uhg = dp_sum(uhg, grad_scale)[0]
    width = jnp.concatenate(width_parts, axis=2)
    dwg = width[0].reshape(nb * chunk, block_size)
    uwg = width[1].reshape(nb * chunk, block_size).T
    return (
        jnp.concatenate(outs, axis=0),
        jnp.concatenate(tgrads, axis=0),
        uwg[None],
        uhg,
        dhg,
        dwg[None],
    )


def solution(mesh):
    in_specs = (
        P("dp", "block"),
        P("dp", "block"),
        P("block", None, None),
        P("block", None, None),
        P("block", None, None),
        P("block", None, None),
    )
    out_specs = in_specs
    return jax.shard_map(shards, mesh=mesh, in_specs=in_specs, out_specs=out_specs, check_vma=False)
```

```python
import math

import jax
import jax.numpy as jnp
from jax import lax
from jax.sharding import PartitionSpec as P

CHUNKS = 2


def gelu_exact(value):
    return 0.5 * value * (1.0 + jax.scipy.special.erf(value / math.sqrt(2.0)))


def gelu_slope(value):
    return 0.5 * (1.0 + jax.scipy.special.erf(value / math.sqrt(2.0))) + value * jnp.exp(
        -0.5 * value * value
    ) / math.sqrt(2.0 * math.pi)


def dot(left, right, left_dims, right_dims, batch=((), ())):
    return lax.dot_general(
        left, right, ((left_dims, right_dims), batch), preferred_element_type=jnp.float32
    )


def pick(pair, index):
    return lax.dynamic_index_in_dim(pair, index, axis=0, keepdims=False)


def dp_sum(grad, scale):
    size = lax.axis_size("dp")
    index = lax.axis_index("dp")
    core = index % 2
    row = index // 2
    core_swap = [(i, i ^ 1) for i in range(size)]
    row_swap = [(i, i ^ 2) for i in range(size)]
    own = (grad * scale).astype(jnp.bfloat16)
    got = lax.ppermute(own, "dp", core_swap)
    pair = (own.astype(jnp.float32) + got.astype(jnp.float32)).astype(jnp.bfloat16)
    pair = pair.reshape((2, grad.shape[0] // 2) + grad.shape[1:])
    mine = pick(pair, core)
    got = lax.ppermute(mine, "dp", row_swap)
    total = (mine.astype(jnp.float32) + got.astype(jnp.float32)).astype(jnp.bfloat16)
    got = lax.ppermute(total, "dp", core_swap)
    full = jnp.where(core == 0, jnp.stack([total, got]), jnp.stack([got, total]))
    return full.astype(jnp.float32).reshape(grad.shape)


def shards(tokens, cotangent, up_width, up_hidden, down_hidden, down_width):
    total_rows, block_size = tokens.shape
    nb = lax.axis_size("block")
    local_blocks = up_hidden.shape[0]
    expand = up_width.shape[2] // block_size
    chunk = local_blocks * expand
    grad_scale = 1.0 / math.sqrt(total_rows * lax.axis_size("dp"))
    uw = up_width[0]
    dw = down_width[0]
    rows = total_rows // CHUNKS

    outs, tgrads = [], []
    dhg = uhg = dwg = uwg = None
    for step in range(CHUNKS):
        x = tokens[step * rows:(step + 1) * rows]
        c = cotangent[step * rows:(step + 1) * rows]
        expanded_t = dot(uw, x, (0,), (1,)).astype(jnp.bfloat16)
        out_grad_t = dot(dw, c, (1,), (1,)).astype(jnp.bfloat16)
        send = jnp.stack(
            [expanded_t.reshape(nb, chunk, rows), out_grad_t.reshape(nb, chunk, rows)], axis=1
        )
        recv = lax.all_to_all(send, "block", 0, 0, tiled=True)
        recv = recv.reshape(nb, 2, local_blocks, expand, rows)
        hidden_t = recv[:, 0].transpose(1, 0, 2, 3).reshape(local_blocks, nb * expand, rows)
        grad_t = recv[:, 1].transpose(1, 0, 2, 3).reshape(local_blocks, nb * expand, rows)

        pre_act = dot(up_hidden, hidden_t, (1,), (1,), ((0,), (0,)))
        active = gelu_exact(pre_act).astype(jnp.bfloat16)
        back_t = dot(down_hidden, active, (1,), (1,), ((0,), (0,))).astype(jnp.bfloat16)
        act_grad = dot(down_hidden, grad_t, (2,), (1,), ((0,), (0,)))
        pre_grad = (act_grad * gelu_slope(pre_act)).astype(jnp.bfloat16)
        tile_grad_t = dot(up_hidden, pre_grad, (2,), (1,), ((0,), (0,))).astype(jnp.bfloat16)
        g_dh = dot(active, grad_t, (2,), (2,), ((0,), (0,)))
        g_uh = dot(hidden_t, pre_grad, (2,), (2,), ((0,), (0,)))
        dhg = g_dh if dhg is None else dhg + g_dh
        uhg = g_uh if uhg is None else uhg + g_uh

        send2 = jnp.stack([back_t, tile_grad_t], axis=0).reshape(2, local_blocks, nb, expand, rows)
        send2 = send2.transpose(2, 0, 1, 3, 4).reshape(nb, 2, chunk, rows)
        recv2 = lax.all_to_all(send2, "block", 0, 0, tiled=True)
        rows_t = recv2[:, 0].reshape(nb * chunk, rows)
        rows_grad_t = recv2[:, 1].reshape(nb * chunk, rows)

        outs.append(dot(rows_t, dw, (0,), (0,)).astype(jnp.bfloat16))
        tgrads.append(dot(rows_grad_t, uw, (0,), (1,)).astype(jnp.bfloat16))
        g_dw = dot(rows_t, c, (1,), (0,))
        g_uw = dot(x, rows_grad_t, (0,), (1,))
        dwg = g_dw if dwg is None else dwg + g_dw
        uwg = g_uw if uwg is None else uwg + g_uw

    hidden_grads = dp_sum(jnp.stack([dhg, uhg]), grad_scale)
    dhg = hidden_grads[0]
    uhg = hidden_grads[1]
    dwg = dp_sum(dwg, grad_scale)
    uwg = dp_sum(uwg, grad_scale)
    return (
        jnp.concatenate(outs, axis=0),
        jnp.concatenate(tgrads, axis=0),
        uwg[None],
        uhg,
        dhg,
        dwg[None],
    )


def solution(mesh):
    in_specs = (
        P("dp", "block"),
        P("dp", "block"),
        P("block", None, None),
        P("block", None, None),
        P("block", None, None),
        P("block", None, None),
    )
    out_specs = in_specs
    return jax.shard_map(shards, mesh=mesh, in_specs=in_specs, out_specs=out_specs, check_vma=False)
```

```python
import math

import jax
import jax.numpy as jnp
from jax import lax
from jax.sharding import PartitionSpec as P

CHUNKS = 2


def gelu_exact(value):
    return 0.5 * value * (1.0 + jax.scipy.special.erf(value / math.sqrt(2.0)))


def gelu_slope(value):
    return 0.5 * (1.0 + jax.scipy.special.erf(value / math.sqrt(2.0))) + value * jnp.exp(
        -0.5 * value * value
    ) / math.sqrt(2.0 * math.pi)


def dot(left, right, left_dims, right_dims, batch=((), ())):
    return lax.dot_general(
        left, right, ((left_dims, right_dims), batch), preferred_element_type=jnp.float32
    )


def pick(pair, index):
    return lax.dynamic_index_in_dim(pair, index, axis=0, keepdims=False)


def dp_sum(grad, scale, tied=None):
    size = lax.axis_size("dp")
    index = lax.axis_index("dp")
    core = index % 2
    row = index // 2
    core_swap = [(i, i ^ 1) for i in range(size)]
    row_swap = [(i, i ^ 2) for i in range(size)]
    own = (grad * scale).astype(jnp.bfloat16)
    got = lax.ppermute(own, "dp", core_swap)
    pair = (own.astype(jnp.float32) + got.astype(jnp.float32)).astype(jnp.bfloat16)
    pair = pair.reshape((2, grad.shape[0] // 2) + grad.shape[1:])
    mine = pick(pair, core)
    if tied is not None:
        mine, tied = lax.optimization_barrier((mine, tied))
    got = lax.ppermute(mine, "dp", row_swap)
    total = (mine.astype(jnp.float32) + got.astype(jnp.float32)).astype(jnp.bfloat16)
    got = lax.ppermute(total, "dp", core_swap)
    full = jnp.zeros((2,) + total.shape, jnp.float32)
    full = lax.dynamic_update_index_in_dim(full, total.astype(jnp.float32), core, 0)
    full = lax.dynamic_update_index_in_dim(full, got.astype(jnp.float32), 1 - core, 0)
    return full.reshape(grad.shape), tied


def shards(tokens, cotangent, up_width, up_hidden, down_hidden, down_width):
    total_rows, block_size = tokens.shape
    nb = lax.axis_size("block")
    local_blocks = up_hidden.shape[0]
    expand = up_width.shape[2] // block_size
    chunk = local_blocks * expand
    grad_scale = 1.0 / math.sqrt(total_rows * lax.axis_size("dp"))
    uw = up_width[0]
    dw = down_width[0]
    rows = total_rows // CHUNKS

    outs, tgrads = [], []
    dhg = uhg = dwg = uwg = None
    for step in range(CHUNKS):
        x = tokens[step * rows:(step + 1) * rows]
        c = cotangent[step * rows:(step + 1) * rows]
        expanded_t = dot(uw, x, (0,), (1,)).astype(jnp.bfloat16)
        out_grad_t = dot(dw, c, (1,), (1,)).astype(jnp.bfloat16)
        send = jnp.stack(
            [expanded_t.reshape(nb, chunk, rows), out_grad_t.reshape(nb, chunk, rows)], axis=1
        )
        recv = lax.all_to_all(send, "block", 0, 0, tiled=True)
        recv = recv.reshape(nb, 2, local_blocks, expand, rows)
        hidden_t = recv[:, 0].transpose(1, 0, 2, 3).reshape(local_blocks, nb * expand, rows)
        grad_t = recv[:, 1].transpose(1, 0, 2, 3).reshape(local_blocks, nb * expand, rows)

        pre_act = dot(up_hidden, hidden_t, (1,), (1,), ((0,), (0,)))
        active = gelu_exact(pre_act).astype(jnp.bfloat16)
        back_t = dot(down_hidden, active, (1,), (1,), ((0,), (0,))).astype(jnp.bfloat16)
        act_grad = dot(down_hidden, grad_t, (2,), (1,), ((0,), (0,)))
        pre_grad = (act_grad * gelu_slope(pre_act)).astype(jnp.bfloat16)
        tile_grad_t = dot(up_hidden, pre_grad, (2,), (1,), ((0,), (0,))).astype(jnp.bfloat16)
        g_dh = dot(active, grad_t, (2,), (2,), ((0,), (0,)))
        g_uh = dot(hidden_t, pre_grad, (2,), (2,), ((0,), (0,)))
        dhg = g_dh if dhg is None else dhg + g_dh
        uhg = g_uh if uhg is None else uhg + g_uh

        send2 = jnp.stack([back_t, tile_grad_t], axis=0).reshape(2, local_blocks, nb, expand, rows)
        send2 = send2.transpose(2, 0, 1, 3, 4).reshape(nb, 2, chunk, rows)
        recv2 = lax.all_to_all(send2, "block", 0, 0, tiled=True)
        rows_t = recv2[:, 0].reshape(nb * chunk, rows)
        rows_grad_t = recv2[:, 1].reshape(nb * chunk, rows)

        if step < CHUNKS - 1:
            outs.append(dot(rows_t, dw, (0,), (0,)).astype(jnp.bfloat16))
            tgrads.append(dot(rows_grad_t, uw, (0,), (1,)).astype(jnp.bfloat16))
        g_dw = dot(rows_t, c, (1,), (0,))
        g_uw = dot(x, rows_grad_t, (0,), (1,))
        dwg = g_dw if dwg is None else dwg + g_dw
        uwg = g_uw if uwg is None else uwg + g_uw

    hidden_grads = dp_sum(jnp.stack([dhg, uhg]), grad_scale)[0]
    dhg = hidden_grads[0]
    uhg = hidden_grads[1]
    dwg, rows_t = dp_sum(dwg, grad_scale, rows_t)
    uwg, rows_grad_t = dp_sum(uwg, grad_scale, rows_grad_t)
    outs.append(dot(rows_t, dw, (0,), (0,)).astype(jnp.bfloat16))
    tgrads.append(dot(rows_grad_t, uw, (0,), (1,)).astype(jnp.bfloat16))
    return (
        jnp.concatenate(outs, axis=0),
        jnp.concatenate(tgrads, axis=0),
        uwg[None],
        uhg,
        dhg,
        dwg[None],
    )


def solution(mesh):
    in_specs = (
        P("dp", "block"),
        P("dp", "block"),
        P("block", None, None),
        P("block", None, None),
        P("block", None, None),
        P("block", None, None),
    )
    out_specs = in_specs
    return jax.shard_map(shards, mesh=mesh, in_specs=in_specs, out_specs=out_specs, check_vma=False)
```

```python
import math

import jax
import jax.numpy as jnp
from jax import lax
from jax.sharding import PartitionSpec as P

CHUNKS = 2


def gelu_exact(value):
    return 0.5 * value * (1.0 + jax.scipy.special.erf(value / math.sqrt(2.0)))


def gelu_slope(value):
    return 0.5 * (1.0 + jax.scipy.special.erf(value / math.sqrt(2.0))) + value * jnp.exp(
        -0.5 * value * value
    ) / math.sqrt(2.0 * math.pi)


def dot(left, right, left_dims, right_dims, batch=((), ())):
    return lax.dot_general(
        left, right, ((left_dims, right_dims), batch), preferred_element_type=jnp.float32
    )


def pick(pair, index):
    return lax.dynamic_index_in_dim(pair, index, axis=0, keepdims=False)


def dp_sum(grad, scale, tied=None):
    size = lax.axis_size("dp")
    index = lax.axis_index("dp")
    core = index % 2
    row = index // 2
    core_swap = [(i, i ^ 1) for i in range(size)]
    row_swap = [(i, i ^ 2) for i in range(size)]
    own = (grad * scale).astype(jnp.bfloat16)
    got = lax.ppermute(own, "dp", core_swap)
    pair = (own.astype(jnp.float32) + got.astype(jnp.float32)).astype(jnp.bfloat16)
    pair = pair.reshape((2, grad.shape[0] // 2) + grad.shape[1:])
    mine = pick(pair, core)
    if tied is not None:
        mine, tied = lax.optimization_barrier((mine, tied))
    got = lax.ppermute(mine, "dp", row_swap)
    total = (mine.astype(jnp.float32) + got.astype(jnp.float32)).astype(jnp.bfloat16)
    got = lax.ppermute(total, "dp", core_swap)
    full = jnp.where(core == 0, jnp.stack([total, got]), jnp.stack([got, total]))
    return full.astype(jnp.float32).reshape(grad.shape), tied


def shards(tokens, cotangent, up_width, up_hidden, down_hidden, down_width):
    total_rows, block_size = tokens.shape
    nb = lax.axis_size("block")
    local_blocks = up_hidden.shape[0]
    expand = up_width.shape[2] // block_size
    chunk = local_blocks * expand
    grad_scale = 1.0 / math.sqrt(total_rows * lax.axis_size("dp"))
    uw = up_width[0]
    dw = down_width[0]
    rows = total_rows // CHUNKS

    outs, tgrads = [], []
    dhg = uhg = dwg = uwg = None
    for step in range(CHUNKS):
        x = tokens[step * rows:(step + 1) * rows]
        c = cotangent[step * rows:(step + 1) * rows]
        expanded_t = dot(uw, x, (0,), (1,)).astype(jnp.bfloat16)
        out_grad_t = dot(dw, c, (1,), (1,)).astype(jnp.bfloat16)
        send = jnp.stack(
            [expanded_t.reshape(nb, chunk, rows), out_grad_t.reshape(nb, chunk, rows)], axis=1
        )
        recv = lax.all_to_all(send, "block", 0, 0, tiled=True)
        recv = recv.reshape(nb, 2, local_blocks, expand, rows)
        hidden_t = recv[:, 0].transpose(1, 0, 2, 3).reshape(local_blocks, nb * expand, rows)
        grad_t = recv[:, 1].transpose(1, 0, 2, 3).reshape(local_blocks, nb * expand, rows)

        pre_act = dot(up_hidden, hidden_t, (1,), (1,), ((0,), (0,)))
        active = gelu_exact(pre_act).astype(jnp.bfloat16)
        back_t = dot(down_hidden, active, (1,), (1,), ((0,), (0,))).astype(jnp.bfloat16)
        act_grad = dot(down_hidden, grad_t, (2,), (1,), ((0,), (0,)))
        pre_grad = (act_grad * gelu_slope(pre_act)).astype(jnp.bfloat16)
        tile_grad_t = dot(up_hidden, pre_grad, (2,), (1,), ((0,), (0,))).astype(jnp.bfloat16)
        g_dh = dot(active, grad_t, (2,), (2,), ((0,), (0,)))
        g_uh = dot(hidden_t, pre_grad, (2,), (2,), ((0,), (0,)))
        dhg = g_dh if dhg is None else dhg + g_dh
        uhg = g_uh if uhg is None else uhg + g_uh

        send2 = jnp.stack([back_t, tile_grad_t], axis=0).reshape(2, local_blocks, nb, expand, rows)
        send2 = send2.transpose(2, 0, 1, 3, 4).reshape(nb, 2, chunk, rows)
        recv2 = lax.all_to_all(send2, "block", 0, 0, tiled=True)
        rows_t = recv2[:, 0].reshape(nb * chunk, rows)
        rows_grad_t = recv2[:, 1].reshape(nb * chunk, rows)

        if step < CHUNKS - 1:
            outs.append(dot(rows_t, dw, (0,), (0,)).astype(jnp.bfloat16))
            tgrads.append(dot(rows_grad_t, uw, (0,), (1,)).astype(jnp.bfloat16))
        g_dw = dot(rows_t, c, (1,), (0,))
        g_uw = dot(x, rows_grad_t, (0,), (1,))
        dwg = g_dw if dwg is None else dwg + g_dw
        uwg = g_uw if uwg is None else uwg + g_uw

    hidden_grads = dp_sum(jnp.stack([dhg, uhg]), grad_scale)[0]
    dhg = hidden_grads[0]
    uhg = hidden_grads[1]
    dwg, rows_t = dp_sum(dwg, grad_scale, rows_t)
    uwg, rows_grad_t = dp_sum(uwg, grad_scale, rows_grad_t)
    outs.append(dot(rows_t, dw, (0,), (0,)).astype(jnp.bfloat16))
    tgrads.append(dot(rows_grad_t, uw, (0,), (1,)).astype(jnp.bfloat16))
    return (
        jnp.concatenate(outs, axis=0),
        jnp.concatenate(tgrads, axis=0),
        uwg[None],
        uhg,
        dhg,
        dwg[None],
    )


def solution(mesh):
    in_specs = (
        P("dp", "block"),
        P("dp", "block"),
        P("block", None, None),
        P("block", None, None),
        P("block", None, None),
        P("block", None, None),
    )
    out_specs = in_specs
    return jax.shard_map(shards, mesh=mesh, in_specs=in_specs, out_specs=out_specs, check_vma=False)
```
